256 devices in a mesh: ta: 8 (over x_lo, y), gx: 4 (over x_hi, core), yz: 8 (over z).
Axes of the slice: x: 4 (x_hi: 2, x_lo: 2; x = x_hi * 2 + x_lo), y: 4, z: 8, core: 2. Of those that a mesh axis runs over, the one named last changes fastest.
Arguments:
- vectors: bfloat16 [2, 3, 32, 64, 256, 128], P(None, None, 'gx', 'yz', 'ta'), parts along dimension 4, may hold values from -6 to 6
- gauge_x: float32 [2, 3, 3, 32, 64, 256], P(None, None, None, 'gx', 'yz', 'ta'), parts along dimension 5, may hold values from -6 to 6
- gauge_y: float32 [2, 3, 3, 32, 64, 256], P(None, None, None, 'gx', 'yz', 'ta'), parts along dimension 5, may hold values from -6 to 6
Outputs:
- elementals: float32 [16, 2, 128, 128], P('ta'), parts along dimension 0
The draws below stay inside these ranges and needn't reach their ends.
There are 8 independent parts, one for each index of `ta`. The reference program is written for one: setup_inputs(seed, part) draws one part's arguments, and reference() takes and returns one part's arrays. A program takes and returns all parts, laid end to end along the dimension named above; each array names one. Nothing has to cross between parts.
All inputs are finite; a program needn't handle non-finite values.
Results may differ from the reference program's by a relative error of at most 0.0029.
Values may be sent and summed in bfloat16 or wider, within the bound.
No kernel may reach another device: no remote copies, remote signals or barrier semaphores. Data moves between devices by JAX's collectives and lax.ppermute only.
A program may use at most 64 MiB of HBM per device.

```python
import math
import jax
import jax.numpy as jnp

NV = 128
LZ = 32
NX = 32
NY = 64


def block_levels(key, shape, shards, least, top_value):
    def one(dim, parts):
        heights = jax.random.uniform(jax.random.fold_in(jax.random.fold_in(key, 6), dim), (parts,), jnp.float32, least / len(shards), top_value / len(shards))
        return jnp.repeat(jnp.exp(heights), shape[dim] // parts).reshape((-1,) + (1,) * (len(shape) - dim - 1))

    loudness = one(*shards[0])
    for cut in shards[1:]:
        loudness = loudness * one(*cut)
    return loudness


def centred(key, shape, width, most, cuts=(), held_as=jnp.bfloat16):
    drawn = jax.random.normal(key, shape, jnp.float32) * width
    if len(cuts) > 0:
        drawn = block_levels(key, shape, cuts, -0.22, 0.18) * drawn
    return jnp.clip(drawn, min=-most, max=most).astype(held_as)


def setup_inputs(seed: int = 0, part: int = 0) -> dict:
    key_list = jax.random.split(jax.random.key(seed), 4)
    part_splits = jax.random.split(jax.random.fold_in(key_list[3], part), 4)
    return {
        "vectors": centred(part_splits[0], (2, 3, NX, NY, LZ, NV), 1.0, 6.0, ((2, 4), (3, 8))),
        "gauge_x": centred(part_splits[1], (2, 3, 3, NX, NY, LZ), 0.4, 6.0, ((3, 4), (4, 8)), jnp.float32),
        "gauge_y": centred(part_splits[2], (2, 3, 3, NX, NY, LZ), 0.4, 6.0, ((3, 4), (4, 8)), jnp.float32),
    }


def colour_apply(gauge, source_vectors):
    real_parts = []
    imag_parts = []
    for colour in range(3):
        real_running = jnp.zeros(source_vectors.shape[2:], jnp.float32)
        imaginary_running = jnp.zeros(source_vectors.shape[2:], jnp.float32)
        for inner_product in range(3):
            left_real = gauge[0, colour, inner_product][..., None]
            left_imaginary = gauge[1, colour, inner_product][..., None]
            right_real = source_vectors[0, inner_product].astype(jnp.float32)
            right_imaginary = source_vectors[1, inner_product].astype(jnp.float32)
            real_running = real_running + left_real * right_real - left_imaginary * right_imaginary
            imaginary_running = imaginary_running + left_real * right_imaginary + left_imaginary * right_real
        real_parts.append(real_running)
        imag_parts.append(imaginary_running)
    return jnp.stack([jnp.stack(real_parts), jnp.stack(imag_parts)]).astype(jnp.bfloat16)

def right_block(image):
    nvecs = image.shape[-1]
    real_rows = image[0].reshape(-1, nvecs)
    imag_rows = image[1].reshape(-1, nvecs)
    first = jnp.concatenate([real_rows, imag_rows], 0)
    second = jnp.concatenate([imag_rows, -real_rows], 0)
    return jnp.concatenate([first, second], 1)

def reference(vectors, gauge_x, gauge_y):
    left_rows = vectors.reshape(-1, NV)
    image_x = colour_apply(gauge_x, jnp.roll(vectors, -1, 2))
    image_y = colour_apply(gauge_y, jnp.roll(vectors, -1, 3))
    right_cols = jnp.concatenate([right_block(image_x), right_block(image_y)], 1)
    partial_value = jnp.dot(left_rows.T, right_cols, preferred_element_type=jnp.float32)
    scaling = 1.0 / math.sqrt(3.0 * NX * NY * LZ)
    return (partial_value * scaling).reshape(NV, 2, 2, NV).transpose(1, 2, 0, 3)
```

```python
import math

import jax
import jax.numpy as jnp
from jax import lax
from jax.sharding import PartitionSpec as P


def shifted(value, axis, steps):
    count = lax.axis_size(axis)
    pairs = [(source, (source + steps) % count) for source in range(count)]
    return lax.ppermute(value, axis, pairs)


def colour_apply(gauge, source_vectors):
    real_parts = []
    imag_parts = []
    for colour in range(3):
        real_running = jnp.zeros(source_vectors.shape[2:], jnp.float32)
        imaginary_running = jnp.zeros(source_vectors.shape[2:], jnp.float32)
        for inner_product in range(3):
            left_real = gauge[0, colour, inner_product][..., None]
            left_imaginary = gauge[1, colour, inner_product][..., None]
            right_real = source_vectors[0, inner_product].astype(jnp.float32)
            right_imaginary = source_vectors[1, inner_product].astype(jnp.float32)
            real_running = real_running + left_real * right_real - left_imaginary * right_imaginary
            imaginary_running = (
                imaginary_running + left_real * right_imaginary + left_imaginary * right_real
            )
        real_parts.append(real_running)
        imag_parts.append(imaginary_running)
    return jnp.stack([jnp.stack(real_parts), jnp.stack(imag_parts)]).astype(jnp.bfloat16)


def right_block(image):
    nvecs = image.shape[-1]
    real_rows = image[0].reshape(-1, nvecs)
    imag_rows = image[1].reshape(-1, nvecs)
    first = jnp.concatenate([real_rows, imag_rows], 0)
    second = jnp.concatenate([imag_rows, -real_rows], 0)
    return (first, second)


def contract(left_cols, right_cols):
    return lax.dot_general(
        left_cols, right_cols, (((0,), (0,)), ((), ())), preferred_element_type=jnp.float32
    )


STEPS = [("gx", 1), ("gx", 2), ("yz", 1), ("yz", 2), ("yz", 4)]

def reduce_partials(x):
    shape = x.shape
    flat = x.reshape(-1)
    bits = []
    for axis, bit in STEPS:
        size = lax.axis_size(axis)
        high = (lax.axis_index(axis) & bit) != 0
        half = flat.shape[0] // 2
        lower, upper = flat[:half], flat[half:]
        keep = jnp.where(high, upper, lower)
        send = jnp.where(high, lower, upper)
        pairs = [(j, j ^ bit) for j in range(size)]
        flat = keep + lax.ppermute(send, axis, pairs)
        bits.append(high)
    for (axis, bit), high in reversed(list(zip(STEPS, bits))):
        size = lax.axis_size(axis)
        pairs = [(j, j ^ bit) for j in range(size)]
        other = lax.ppermute(flat, axis, pairs)
        flat = jnp.where(high, jnp.concatenate([other, flat]), jnp.concatenate([flat, other]))
    return flat.reshape(shape)


def local(vectors, gauge_x, gauge_y):
    nvecs = vectors.shape[-1]
    from_next_x = shifted(vectors[:, :, :1], "gx", -1)
    shifted_x = jnp.concatenate([vectors[:, :, 1:], from_next_x], 2)
    from_next_y = shifted(vectors[:, :, :, :1], "yz", -1)
    shifted_y = jnp.concatenate([vectors[:, :, :, 1:], from_next_y], 3)
    image_x = colour_apply(gauge_x, shifted_x)
    image_y = colour_apply(gauge_y, shifted_y)
    left_rows = vectors.reshape(-1, nvecs)
    blocks = right_block(image_x) + right_block(image_y)
    summed = reduce_partials(jnp.concatenate([contract(left_rows, member) for member in blocks], 1))
    sites_total = (
        vectors.shape[2]
        * lax.axis_size("gx")
        * vectors.shape[3]
        * lax.axis_size("yz")
        * vectors.shape[4]
    )
    scaling = 1.0 / math.sqrt(3.0 * sites_total)
    return (summed * scaling).reshape(nvecs, 2, 2, nvecs).transpose(1, 2, 0, 3)


def solution(mesh):
    placed = (
        P(None, None, "gx", "yz", "ta", None),
        P(None, None, None, "gx", "yz", "ta"),
        P(None, None, None, "gx", "yz", "ta"),
    )
    return jax.shard_map(
        local, mesh=mesh, in_specs=placed, out_specs=P("ta", None, None, None), check_vma=False
    )
```

```python
import math

import jax
import jax.numpy as jnp
from jax import lax
from jax.sharding import PartitionSpec as P


def shifted(value, axis, steps):
    count = lax.axis_size(axis)
    pairs = [(source, (source + steps) % count) for source in range(count)]
    return lax.ppermute(value, axis, pairs)


def colour_apply(gauge, source_vectors):
    real_parts = []
    imag_parts = []
    for colour in range(3):
        real_running = jnp.zeros(source_vectors.shape[2:], jnp.float32)
        imaginary_running = jnp.zeros(source_vectors.shape[2:], jnp.float32)
        for inner_product in range(3):
            left_real = gauge[0, colour, inner_product][..., None]
            left_imaginary = gauge[1, colour, inner_product][..., None]
            right_real = source_vectors[0, inner_product].astype(jnp.float32)
            right_imaginary = source_vectors[1, inner_product].astype(jnp.float32)
            real_running = real_running + left_real * right_real - left_imaginary * right_imaginary
            imaginary_running = (
                imaginary_running + left_real * right_imaginary + left_imaginary * right_real
            )
        real_parts.append(real_running)
        imag_parts.append(imaginary_running)
    return jnp.stack([jnp.stack(real_parts), jnp.stack(imag_parts)]).astype(jnp.bfloat16)


def right_block(image):
    nvecs = image.shape[-1]
    real_rows = image[0].reshape(-1, nvecs)
    imag_rows = image[1].reshape(-1, nvecs)
    first = jnp.concatenate([real_rows, imag_rows], 0)
    second = jnp.concatenate([imag_rows, -real_rows], 0)
    return (first, second)


def contract(left_cols, right_cols):
    return lax.dot_general(
        left_cols, right_cols, (((0,), (0,)), ((), ())), preferred_element_type=jnp.float32
    )


def reduce_partials(x):
    shape = x.shape
    n = lax.axis_size("gx") * lax.axis_size("yz")
    chunks = x.reshape(n, -1)
    got = lax.all_to_all(chunks, ("gx", "yz"), 0, 0, tiled=True)
    total = jnp.sum(got, 0, keepdims=True)
    every = jnp.broadcast_to(total, (n, total.shape[1]))
    return lax.all_to_all(every, ("gx", "yz"), 0, 0, tiled=True).reshape(shape)


def local(vectors, gauge_x, gauge_y):
    nvecs = vectors.shape[-1]
    from_next_x = shifted(vectors[:, :, :1], "gx", -1)
    shifted_x = jnp.concatenate([vectors[:, :, 1:], from_next_x], 2)
    from_next_y = shifted(vectors[:, :, :, :1], "yz", -1)
    shifted_y = jnp.concatenate([vectors[:, :, :, 1:], from_next_y], 3)
    image_x = colour_apply(gauge_x, shifted_x)
    image_y = colour_apply(gauge_y, shifted_y)
    left_rows = vectors.reshape(-1, nvecs)
    blocks = right_block(image_x) + right_block(image_y)
    summed = reduce_partials(jnp.concatenate([contract(left_rows, member) for member in blocks], 1))
    sites_total = (
        vectors.shape[2]
        * lax.axis_size("gx")
        * vectors.shape[3]
        * lax.axis_size("yz")
        * vectors.shape[4]
    )
    scaling = 1.0 / math.sqrt(3.0 * sites_total)
    return (summed * scaling).reshape(nvecs, 2, 2, nvecs).transpose(1, 2, 0, 3)


def solution(mesh):
    placed = (
        P(None, None, "gx", "yz", "ta", None),
        P(None, None, None, "gx", "yz", "ta"),
        P(None, None, None, "gx", "yz", "ta"),
    )
    return jax.shard_map(
        local, mesh=mesh, in_specs=placed, out_specs=P("ta", None, None, None), check_vma=False
    )
```

```python
import math

import jax
import jax.numpy as jnp
from jax import lax
from jax.experimental import pallas as pl
from jax.experimental.pallas import tpu as pltpu
from jax.sharding import PartitionSpec as P


def shifted(value, axis, steps):
    count = lax.axis_size(axis)
    pairs = [(source, (source + steps) % count) for source in range(count)]
    return lax.ppermute(value, axis, pairs)


def elementals_kernel(scaling, v_ref, hx_ref, hy_ref, g_ref, o_ref, vt_ref, wy_ref, r_ref, acc_a, acc_b):
    planes, lines, row, vecs = v_ref.shape[2:]
    sites = lines * row
    step = 16
    nt = (((1,), (1,)), ((), ()))

    def transpose_plane(p, carry):
        for c in range(2):
            for a in range(3):
                vt_ref[c, a, p] = v_ref[c, a, p].reshape(sites, vecs).T
                inner = v_ref[c, a, p, 1:].reshape(sites - row, vecs)
                wy_ref[c, a, p] = jnp.concatenate([inner, hy_ref[c, a, p, 0]], 0).T
        return carry

    lax.fori_loop(0, planes, transpose_plane, 0)
    for c in range(2):
        for a in range(3):
            vt_ref[c, a, planes] = hx_ref[c, a, 0].reshape(sites, vecs).T
    acc_a[...] = jnp.zeros_like(acc_a)
    acc_b[...] = jnp.zeros_like(acc_b)

    def plane(p, carry):
        def rows_block(jc, inner_carry):
            j0 = pl.multiple_of(jc * step, step)
            sources = (
                lambda c, b: vt_ref[c, b, p + 1, pl.ds(j0, step), :],
                lambda c, b: wy_ref[c, b, p, pl.ds(j0, step), :],
            )
            for d in range(2):
                w_re = [sources[d](0, b).astype(jnp.float32) for b in range(3)]
                w_im = [sources[d](1, b).astype(jnp.float32) for b in range(3)]
                for a in range(3):
                    re = None
                    im = None
                    for b in range(3):
                        k = d * 18 + a * 3 + b
                        gr = g_ref[p, k : k + 1, :]
                        gi = g_ref[p, k + 9 : k + 10, :]
                        t_re = gr * w_re[b] - gi * w_im[b]
                        t_im = gr * w_im[b] + gi * w_re[b]
                        re = t_re if re is None else re + t_re
                        im = t_im if im is None else im + t_im
                    r_ref[a, pl.ds(2 * d * vecs + j0, step), :] = re.astype(jnp.bfloat16)
                    r_ref[a, pl.ds((2 * d + 1) * vecs + j0, step), :] = im.astype(jnp.bfloat16)
            return inner_carry

        lax.fori_loop(0, vecs // step, rows_block, 0)
        for a in range(3):
            right = r_ref[a]
            acc_a[...] += lax.dot_general(vt_ref[0, a, p], right, nt, preferred_element_type=jnp.float32)
            acc_b[...] += lax.dot_general(vt_ref[1, a, p], right, nt, preferred_element_type=jnp.float32)
        return carry

    lax.fori_loop(0, planes, plane, 0)
    a = acc_a[...]
    b = acc_b[...]
    for d in range(2):
        o = 2 * d * vecs
        o_ref[d, 0] = (a[:, o : o + vecs] + b[:, o + vecs : o + 2 * vecs]) * scaling
        o_ref[d, 1] = (a[:, o + vecs : o + 2 * vecs] - b[:, o : o + vecs]) * scaling


def site_rows(gauge_x, gauge_y):
    nx, ny, nz = gauge_x.shape[3:]
    both = jnp.concatenate([gauge_x.reshape(18, nx, ny * nz), gauge_y.reshape(18, nx, ny * nz)], 0)
    return jnp.transpose(both, (1, 0, 2))


def partials(vectors, from_next_x, from_next_y, gauge_x, gauge_y, scaling):
    nx, ny, nz, nv = vectors.shape[2:]
    sites = ny * nz
    vmem = pltpu.MemorySpace.VMEM
    return pl.pallas_call(
        lambda *refs: elementals_kernel(scaling, *refs),
        out_shape=jax.ShapeDtypeStruct((2, 2, nv, nv), jnp.float32),
        in_specs=[pl.BlockSpec(memory_space=vmem)] * 4,
        out_specs=pl.BlockSpec(memory_space=vmem),
        scratch_shapes=[
            pltpu.VMEM((2, 3, nx + 1, nv, sites), jnp.bfloat16),
            pltpu.VMEM((2, 3, nx, nv, sites), jnp.bfloat16),
            pltpu.VMEM((3, 4 * nv, sites), jnp.bfloat16),
            pltpu.VMEM((nv, 4 * nv), jnp.float32),
            pltpu.VMEM((nv, 4 * nv), jnp.float32),
        ],
    )(vectors, from_next_x, from_next_y, site_rows(gauge_x, gauge_y))


def reduce_partials(x):
    shape = x.shape
    n = lax.axis_size("gx") * lax.axis_size("yz")
    chunks = x.reshape(n, -1, shape[-1])
    got = lax.all_to_all(chunks, ("gx", "yz"), 0, 0, tiled=True)
    total = jnp.sum(got, 0, keepdims=True)
    every = jnp.broadcast_to(total, chunks.shape)
    return lax.all_to_all(every, ("gx", "yz"), 0, 0, tiled=True).reshape(shape)


def local(vectors, gauge_x, gauge_y):
    from_next_x = shifted(vectors[:, :, :1], "gx", -1)
    from_next_y = shifted(vectors[:, :, :, :1], "yz", -1)
    sites_total = (
        vectors.shape[2]
        * lax.axis_size("gx")
        * vectors.shape[3]
        * lax.axis_size("yz")
        * vectors.shape[4]
    )
    scaling = 1.0 / math.sqrt(3.0 * sites_total)
    return reduce_partials(partials(vectors, from_next_x, from_next_y, gauge_x, gauge_y, scaling))


def solution(mesh):
    placed = (
        P(None, None, "gx", "yz", "ta", None),
        P(None, None, None, "gx", "yz", "ta"),
        P(None, None, None, "gx", "yz", "ta"),
    )
    return jax.shard_map(
        local, mesh=mesh, in_specs=placed, out_specs=P("ta", None, None, None), check_vma=False
    )
```

```python
import math

import jax
import jax.numpy as jnp
from jax import lax
from jax.experimental import pallas as pl
from jax.experimental.pallas import tpu as pltpu
from jax.sharding import PartitionSpec as P


def shifted(value, axis, steps):
    count = lax.axis_size(axis)
    pairs = [(source, (source + steps) % count) for source in range(count)]
    return lax.ppermute(value, axis, pairs)


def elementals_kernel(scaling, v_ref, hx_ref, hy_ref, g_ref, o_ref, vt_ref, wy_ref, r_ref):
    planes, lines, row, vecs = v_ref.shape[2:]
    sites = lines * row
    span = 3 * sites
    step = 16
    nt = (((1,), (1,)), ((), ()))

    def lanes(p, a):
        return pl.ds(pl.multiple_of(p * span + a * sites, sites), sites)

    def transpose_plane(p, carry):
        for c in range(2):
            for a in range(3):
                vt_ref[c, :, lanes(p, a)] = v_ref[c, a, p].reshape(sites, vecs).T
                inner = v_ref[c, a, p, 1:].reshape(sites - row, vecs)
                wy_ref[c, a, p] = jnp.concatenate([inner, hy_ref[c, a, p, 0]], 0).T
        return carry

    lax.fori_loop(0, planes, transpose_plane, 0)
    for c in range(2):
        for a in range(3):
            vt_ref[c, :, lanes(planes, a)] = hx_ref[c, a, 0].reshape(sites, vecs).T

    def plane(p, carry):
        def rows_block(jc, inner_carry):
            j0 = pl.multiple_of(jc * step, step)
            sources = (
                lambda c, b: vt_ref[c, pl.ds(j0, step), lanes(p + 1, b)],
                lambda c, b: wy_ref[c, b, p, pl.ds(j0, step), :],
            )
            for d in range(2):
                w_re = [sources[d](0, b).astype(jnp.float32) for b in range(3)]
                w_im = [sources[d](1, b).astype(jnp.float32) for b in range(3)]
                for a in range(3):
                    re = None
                    im = None
                    for b in range(3):
                        k = d * 18 + a * 3 + b
                        gr = g_ref[p, k : k + 1, :]
                        gi = g_ref[p, k + 9 : k + 10, :]
                        t_re = gr * w_re[b] - gi * w_im[b]
                        t_im = gr * w_im[b] + gi * w_re[b]
                        re = t_re if re is None else re + t_re
                        im = t_im if im is None else im + t_im
                    r_ref[pl.ds(2 * d * vecs + j0, step), lanes(p, a)] = re.astype(jnp.bfloat16)
                    r_ref[pl.ds((2 * d + 1) * vecs + j0, step), lanes(p, a)] = im.astype(jnp.bfloat16)
            return inner_carry

        lax.fori_loop(0, vecs // step, rows_block, 0)
        return carry

    lax.fori_loop(0, planes, plane, 0)
    used = planes * span
    right = r_ref[...]
    a = lax.dot_general(vt_ref[0, :, 0:used], right, nt, preferred_element_type=jnp.float32)
    b = lax.dot_general(vt_ref[1, :, 0:used], right, nt, preferred_element_type=jnp.float32)
    for d in range(2):
        o = 2 * d * vecs
        o_ref[d, 0] = (a[:, o : o + vecs] + b[:, o + vecs : o + 2 * vecs]) * scaling
        o_ref[d, 1] = (a[:, o + vecs : o + 2 * vecs] - b[:, o : o + vecs]) * scaling


def site_rows(gauge_x, gauge_y):
    nx, ny, nz = gauge_x.shape[3:]
    both = jnp.concatenate([gauge_x.reshape(18, nx, ny * nz), gauge_y.reshape(18, nx, ny * nz)], 0)
    return jnp.transpose(both, (1, 0, 2))


def partials(vectors, from_next_x, from_next_y, gauge_x, gauge_y, scaling):
    nx, ny, nz, nv = vectors.shape[2:]
    sites = ny * nz
    vmem = pltpu.MemorySpace.VMEM
    return pl.pallas_call(
        lambda *refs: elementals_kernel(scaling, *refs),
        out_shape=jax.ShapeDtypeStruct((2, 2, nv, nv), jnp.float32),
        in_specs=[pl.BlockSpec(memory_space=vmem)] * 4,
        out_specs=pl.BlockSpec(memory_space=vmem),
        scratch_shapes=[
            pltpu.VMEM((2, nv, (nx + 1) * 3 * sites), jnp.bfloat16),
            pltpu.VMEM((2, 3, nx, nv, sites), jnp.bfloat16),
            pltpu.VMEM((4 * nv, nx * 3 * sites), jnp.bfloat16),
        ],
    )(vectors, from_next_x, from_next_y, site_rows(gauge_x, gauge_y))


def reduce_partials(x):
    shape = x.shape
    n = lax.axis_size("gx") * lax.axis_size("yz")
    chunks = x.reshape(n, -1, shape[-1])
    got = lax.all_to_all(chunks, ("gx", "yz"), 0, 0, tiled=True)
    total = jnp.sum(got, 0, keepdims=True)
    every = jnp.broadcast_to(total, chunks.shape)
    return lax.all_to_all(every, ("gx", "yz"), 0, 0, tiled=True).reshape(shape)


def local(vectors, gauge_x, gauge_y):
    from_next_x = shifted(vectors[:, :, :1], "gx", -1)
    from_next_y = shifted(vectors[:, :, :, :1], "yz", -1)
    sites_total = (
        vectors.shape[2]
        * lax.axis_size("gx")
        * vectors.shape[3]
        * lax.axis_size("yz")
        * vectors.shape[4]
    )
    scaling = 1.0 / math.sqrt(3.0 * sites_total)
    return reduce_partials(partials(vectors, from_next_x, from_next_y, gauge_x, gauge_y, scaling))


def solution(mesh):
    placed = (
        P(None, None, "gx", "yz", "ta", None),
        P(None, None, None, "gx", "yz", "ta"),
        P(None, None, None, "gx", "yz", "ta"),
    )
    return jax.shard_map(
        local, mesh=mesh, in_specs=placed, out_specs=P("ta", None, None, None), check_vma=False
    )
```

```python
import math

import jax
import jax.numpy as jnp
from jax import lax
from jax.experimental import pallas as pl
from jax.experimental.pallas import tpu as pltpu
from jax.sharding import PartitionSpec as P


def shifted(value, axis, steps):
    count = lax.axis_size(axis)
    pairs = [(source, (source + steps) % count) for source in range(count)]
    return lax.ppermute(value, axis, pairs)


def elementals_kernel(scaling, v_ref, hx_ref, g_ref, o_ref, vt_ref, wy_ref, r_ref):
    planes, lines, row, vecs = v_ref.shape[2:]
    sites = lines * row
    span = 3 * sites
    step = 16
    nt = (((1,), (1,)), ((), ()))

    def lanes(p, a):
        return pl.ds(pl.multiple_of(p * span + a * sites, sites), sites)

    def transpose_plane(p, carry):
        for c in range(2):
            for a in range(3):
                vt_ref[c, :, lanes(p, a)] = v_ref[c, a, p].reshape(sites, vecs).T
                inner = v_ref[c, a, p, 1:].reshape(sites - row, vecs)
                edge = jnp.zeros((row, vecs), inner.dtype)
                wy_ref[c, a, p] = jnp.concatenate([inner, edge], 0).T
        return carry

    lax.fori_loop(0, planes, transpose_plane, 0)
    for c in range(2):
        for a in range(3):
            vt_ref[c, :, lanes(planes, a)] = hx_ref[c, a, 0].reshape(sites, vecs).T

    def plane(p, carry):
        def rows_block(jc, inner_carry):
            j0 = pl.multiple_of(jc * step, step)
            sources = (
                lambda c, b: vt_ref[c, pl.ds(j0, step), lanes(p + 1, b)],
                lambda c, b: wy_ref[c, b, p, pl.ds(j0, step), :],
            )
            for d in range(2):
                w_re = [sources[d](0, b).astype(jnp.float32) for b in range(3)]
                w_im = [sources[d](1, b).astype(jnp.float32) for b in range(3)]
                for a in range(3):
                    re = None
                    im = None
                    for b in range(3):
                        k = d * 18 + a * 3 + b
                        gr = g_ref[p, k : k + 1, :]
                        gi = g_ref[p, k + 9 : k + 10, :]
                        t_re = gr * w_re[b] - gi * w_im[b]
                        t_im = gr * w_im[b] + gi * w_re[b]
                        re = t_re if re is None else re + t_re
                        im = t_im if im is None else im + t_im
                    r_ref[pl.ds(2 * d * vecs + j0, step), lanes(p, a)] = re.astype(jnp.bfloat16)
                    r_ref[pl.ds((2 * d + 1) * vecs + j0, step), lanes(p, a)] = im.astype(jnp.bfloat16)
            return inner_carry

        lax.fori_loop(0, vecs // step, rows_block, 0)
        return carry

    lax.fori_loop(0, planes, plane, 0)
    used = planes * span
    right = r_ref[...]
    a = lax.dot_general(vt_ref[0, :, 0:used], right, nt, preferred_element_type=jnp.float32)
    b = lax.dot_general(vt_ref[1, :, 0:used], right, nt, preferred_element_type=jnp.float32)
    for d in range(2):
        o = 2 * d * vecs
        o_ref[d, 0] = (a[:, o : o + vecs] + b[:, o + vecs : o + 2 * vecs]) * scaling
        o_ref[d, 1] = (a[:, o + vecs : o + 2 * vecs] - b[:, o : o + vecs]) * scaling


def site_rows(gauge_x, gauge_y):
    nx, ny, nz = gauge_x.shape[3:]
    both = jnp.concatenate([gauge_x.reshape(18, nx, ny * nz), gauge_y.reshape(18, nx, ny * nz)], 0)
    return jnp.transpose(both, (1, 0, 2))


def partials(vectors, from_next_x, from_next_y, gauge_x, gauge_y, scaling):
    nx, ny, nz, nv = vectors.shape[2:]
    sites = ny * nz
    vmem = pltpu.MemorySpace.VMEM
    inner = pl.pallas_call(
        lambda *refs: elementals_kernel(scaling, *refs),
        out_shape=jax.ShapeDtypeStruct((2, 2, nv, nv), jnp.float32),
        in_specs=[pl.BlockSpec(memory_space=vmem)] * 3,
        out_specs=pl.BlockSpec(memory_space=vmem),
        scratch_shapes=[
            pltpu.VMEM((2, nv, (nx + 1) * 3 * sites), jnp.bfloat16),
            pltpu.VMEM((2, 3, nx, nv, sites), jnp.bfloat16),
            pltpu.VMEM((4 * nv, nx * 3 * sites), jnp.bfloat16),
        ],
    )(vectors, from_next_x, site_rows(gauge_x, gauge_y))
    inner, from_next_y = lax.optimization_barrier((inner, from_next_y))
    return inner + last_line_term(vectors, from_next_y, gauge_y, scaling)


def colour_apply(gauge, source_vectors):
    real_parts = []
    imag_parts = []
    for colour in range(3):
        real_running = jnp.zeros(source_vectors.shape[2:], jnp.float32)
        imaginary_running = jnp.zeros(source_vectors.shape[2:], jnp.float32)
        for inner_product in range(3):
            left_real = gauge[0, colour, inner_product][..., None]
            left_imaginary = gauge[1, colour, inner_product][..., None]
            right_real = source_vectors[0, inner_product].astype(jnp.float32)
            right_imaginary = source_vectors[1, inner_product].astype(jnp.float32)
            real_running = real_running + left_real * right_real - left_imaginary * right_imaginary
            imaginary_running = (
                imaginary_running + left_real * right_imaginary + left_imaginary * right_real
            )
        real_parts.append(real_running)
        imag_parts.append(imaginary_running)
    return jnp.stack([jnp.stack(real_parts), jnp.stack(imag_parts)]).astype(jnp.bfloat16)


def last_line_term(vectors, from_next_y, gauge_y, scaling):
    lines = vectors.shape[3]
    nv = vectors.shape[-1]
    image = colour_apply(gauge_y[:, :, :, :, lines - 1 :], from_next_y)
    left = vectors[:, :, :, lines - 1 :].reshape(-1, nv)
    right_re = image[0].reshape(-1, nv)
    right_im = image[1].reshape(-1, nv)
    right = jnp.concatenate(
        [jnp.concatenate([right_re, right_im], 1), jnp.concatenate([right_im, -right_re], 1)], 0
    )
    dims = (((0,), (0,)), ((), ()))
    both = lax.dot_general(left, right, dims, preferred_element_type=jnp.float32)
    term = both.reshape(nv, 2, nv).transpose(1, 0, 2) * scaling
    return jnp.stack([jnp.zeros_like(term), term])


def reduce_partials(x):
    shape = x.shape
    n = lax.axis_size("gx") * lax.axis_size("yz")
    chunks = x.reshape(n, -1, shape[-1])
    got = lax.all_to_all(chunks, ("gx", "yz"), 0, 0, tiled=True)
    total = jnp.sum(got, 0, keepdims=True)
    every = jnp.broadcast_to(total, chunks.shape)
    return lax.all_to_all(every, ("gx", "yz"), 0, 0, tiled=True).reshape(shape)


def local(vectors, gauge_x, gauge_y):
    from_next_x = shifted(vectors[:, :, :1], "gx", -1)
    from_next_y = shifted(vectors[:, :, :, :1], "yz", -1)
    sites_total = (
        vectors.shape[2]
        * lax.axis_size("gx")
        * vectors.shape[3]
        * lax.axis_size("yz")
        * vectors.shape[4]
    )
    scaling = 1.0 / math.sqrt(3.0 * sites_total)
    return reduce_partials(partials(vectors, from_next_x, from_next_y, gauge_x, gauge_y, scaling))


def solution(mesh):
    placed = (
        P(None, None, "gx", "yz", "ta", None),
        P(None, None, None, "gx", "yz", "ta"),
        P(None, None, None, "gx", "yz", "ta"),
    )
    return jax.shard_map(
        local, mesh=mesh, in_specs=placed, out_specs=P("ta", None, None, None), check_vma=False
    )
```

```python
import math

import jax
import jax.numpy as jnp
from jax import lax
from jax.experimental import pallas as pl
from jax.experimental.pallas import tpu as pltpu
from jax.sharding import PartitionSpec as P


def shifted(value, axis, steps):
    count = lax.axis_size(axis)
    pairs = [(source, (source + steps) % count) for source in range(count)]
    return lax.ppermute(value, axis, pairs)


def elementals_kernel(scaling, v_ref, g_ref, o_ref, vt_ref, wy_ref, r_ref):
    planes, lines, row, vecs = v_ref.shape[2:]
    sites = lines * row
    span = 3 * sites
    step = 16
    nt = (((1,), (1,)), ((), ()))

    def lanes(p, a):
        return pl.ds(pl.multiple_of(p * span + a * sites, sites), sites)

    def transpose_plane(p, carry):
        for c in range(2):
            for a in range(3):
                vt_ref[c, :, lanes(p, a)] = v_ref[c, a, p].reshape(sites, vecs).T
                inner = v_ref[c, a, p, 1:].reshape(sites - row, vecs)
                edge = jnp.zeros((row, vecs), inner.dtype)
                wy_ref[c, a, p] = jnp.concatenate([inner, edge], 0).T
        return carry

    lax.fori_loop(0, planes, transpose_plane, 0)
    for c in range(2):
        for a in range(3):
            vt_ref[c, :, lanes(planes, a)] = jnp.zeros((vecs, sites), vt_ref.dtype)

    def plane(p, carry):
        def rows_block(jc, inner_carry):
            j0 = pl.multiple_of(jc * step, step)
            sources = (
                lambda c, b: vt_ref[c, pl.ds(j0, step), lanes(p + 1, b)],
                lambda c, b: wy_ref[c, b, p, pl.ds(j0, step), :],
            )
            for d in range(2):
                w_re = [sources[d](0, b).astype(jnp.float32) for b in range(3)]
                w_im = [sources[d](1, b).astype(jnp.float32) for b in range(3)]
                for a in range(3):
                    re = None
                    im = None
                    for b in range(3):
                        k = d * 18 + a * 3 + b
                        gr = g_ref[p, k : k + 1, :]
                        gi = g_ref[p, k + 9 : k + 10, :]
                        t_re = gr * w_re[b] - gi * w_im[b]
                        t_im = gr * w_im[b] + gi * w_re[b]
                        re = t_re if re is None else re + t_re
                        im = t_im if im is None else im + t_im
                    r_ref[pl.ds(2 * d * vecs + j0, step), lanes(p, a)] = re.astype(jnp.bfloat16)
                    r_ref[pl.ds((2 * d + 1) * vecs + j0, step), lanes(p, a)] = im.astype(jnp.bfloat16)
            return inner_carry

        lax.fori_loop(0, vecs // step, rows_block, 0)
        return carry

    lax.fori_loop(0, planes, plane, 0)
    used = planes * span
    right = r_ref[...]
    a = lax.dot_general(vt_ref[0, :, 0:used], right, nt, preferred_element_type=jnp.float32)
    b = lax.dot_general(vt_ref[1, :, 0:used], right, nt, preferred_element_type=jnp.float32)
    for d in range(2):
        o = 2 * d * vecs
        o_ref[d, 0] = (a[:, o : o + vecs] + b[:, o + vecs : o + 2 * vecs]) * scaling
        o_ref[d, 1] = (a[:, o + vecs : o + 2 * vecs] - b[:, o : o + vecs]) * scaling


def site_rows(gauge_x, gauge_y):
    nx, ny, nz = gauge_x.shape[3:]
    both = jnp.concatenate([gauge_x.reshape(18, nx, ny * nz), gauge_y.reshape(18, nx, ny * nz)], 0)
    return jnp.transpose(both, (1, 0, 2))


def partials(vectors, from_next_x, from_next_y, gauge_x, gauge_y, scaling):
    nx, ny, nz, nv = vectors.shape[2:]
    sites = ny * nz
    vmem = pltpu.MemorySpace.VMEM
    inner = pl.pallas_call(
        lambda *refs: elementals_kernel(scaling, *refs),
        out_shape=jax.ShapeDtypeStruct((2, 2, nv, nv), jnp.float32),
        in_specs=[pl.BlockSpec(memory_space=vmem)] * 2,
        out_specs=pl.BlockSpec(memory_space=vmem),
        scratch_shapes=[
            pltpu.VMEM((2, nv, (nx + 1) * 3 * sites), jnp.bfloat16),
            pltpu.VMEM((2, 3, nx, nv, sites), jnp.bfloat16),
            pltpu.VMEM((4 * nv, nx * 3 * sites), jnp.bfloat16),
        ],
    )(vectors, site_rows(gauge_x, gauge_y))
    inner, from_next_x, from_next_y = lax.optimization_barrier((inner, from_next_x, from_next_y))
    edges = jnp.stack(
        [
            last_term(vectors[:, :, nx - 1 :], from_next_x, gauge_x[:, :, :, nx - 1 :], scaling),
            last_term(vectors[:, :, :, ny - 1 :], from_next_y, gauge_y[:, :, :, :, ny - 1 :], scaling),
        ]
    )
    return inner + edges


def colour_apply(gauge, source_vectors):
    real_parts = []
    imag_parts = []
    for colour in range(3):
        real_running = jnp.zeros(source_vectors.shape[2:], jnp.float32)
        imaginary_running = jnp.zeros(source_vectors.shape[2:], jnp.float32)
        for inner_product in range(3):
            left_real = gauge[0, colour, inner_product][..., None]
            left_imaginary = gauge[1, colour, inner_product][..., None]
            right_real = source_vectors[0, inner_product].astype(jnp.float32)
            right_imaginary = source_vectors[1, inner_product].astype(jnp.float32)
            real_running = real_running + left_real * right_real - left_imaginary * right_imaginary
            imaginary_running = (
                imaginary_running + left_real * right_imaginary + left_imaginary * right_real
            )
        real_parts.append(real_running)
        imag_parts.append(imaginary_running)
    return jnp.stack([jnp.stack(real_parts), jnp.stack(imag_parts)]).astype(jnp.bfloat16)


def last_term(left_vectors, source, gauge, scaling):
    nv = left_vectors.shape[-1]
    image = colour_apply(gauge, source)
    left = left_vectors.reshape(-1, nv)
    right_re = image[0].reshape(-1, nv)
    right_im = image[1].reshape(-1, nv)
    right = jnp.concatenate(
        [jnp.concatenate([right_re, right_im], 1), jnp.concatenate([right_im, -right_re], 1)], 0
    )
    dims = (((0,), (0,)), ((), ()))
    both = lax.dot_general(left, right, dims, preferred_element_type=jnp.float32)
    return both.reshape(nv, 2, nv).transpose(1, 0, 2) * scaling


def reduce_partials(x):
    shape = x.shape
    n = lax.axis_size("gx") * lax.axis_size("yz")
    chunks = x.reshape(n, -1, shape[-1])
    got = lax.all_to_all(chunks, ("gx", "yz"), 0, 0, tiled=True)
    total = jnp.sum(got, 0, keepdims=True)
    every = jnp.broadcast_to(total, chunks.shape)
    return lax.all_to_all(every, ("gx", "yz"), 0, 0, tiled=True).reshape(shape)


def local(vectors, gauge_x, gauge_y):
    from_next_x = shifted(vectors[:, :, :1], "gx", -1)
    from_next_y = shifted(vectors[:, :, :, :1], "yz", -1)
    sites_total = (
        vectors.shape[2]
        * lax.axis_size("gx")
        * vectors.shape[3]
        * lax.axis_size("yz")
        * vectors.shape[4]
    )
    scaling = 1.0 / math.sqrt(3.0 * sites_total)
    return reduce_partials(partials(vectors, from_next_x, from_next_y, gauge_x, gauge_y, scaling))


def solution(mesh):
    placed = (
        P(None, None, "gx", "yz", "ta", None),
        P(None, None, None, "gx", "yz", "ta"),
        P(None, None, None, "gx", "yz", "ta"),
    )
    return jax.shard_map(
        local, mesh=mesh, in_specs=placed, out_specs=P("ta", None, None, None), check_vma=False
    )
```

```python
import math

import jax
import jax.numpy as jnp
from jax import lax
from jax.experimental import pallas as pl
from jax.experimental.pallas import tpu as pltpu
from jax.sharding import PartitionSpec as P


def shifted(value, axis, steps):
    count = lax.axis_size(axis)
    pairs = [(source, (source + steps) % count) for source in range(count)]
    return lax.ppermute(value, axis, pairs)


def elementals_kernel(scaling, v_ref, g_ref, o_ref, vt_ref, wy_ref, r_ref):
    planes, lines, row, vecs = v_ref.shape[2:]
    sites = lines * row
    span = 3 * sites
    step = 16
    nt = (((1,), (1,)), ((), ()))

    def lanes(p, a):
        return pl.ds(pl.multiple_of(p * span + a * sites, sites), sites)

    def transpose_plane(p, carry):
        for c in range(2):
            for a in range(3):
                vt_ref[c, :, lanes(p, a)] = v_ref[c, a, p].reshape(sites, vecs).T
                inner = v_ref[c, a, p, 1:].reshape(sites - row, vecs)
                edge = jnp.zeros((row, vecs), inner.dtype)
                wy_ref[c, a, p] = jnp.concatenate([inner, edge], 0).T
        return carry

    lax.fori_loop(0, planes, transpose_plane, 0)
    for c in range(2):
        for a in range(3):
            vt_ref[c, :, lanes(planes, a)] = jnp.zeros((vecs, sites), vt_ref.dtype)

    def plane(p, carry):
        def rows_block(jc, inner_carry):
            j0 = pl.multiple_of(jc * step, step)
            sources = (
                lambda c, b: vt_ref[c, pl.ds(j0, step), lanes(p + 1, b)],
                lambda c, b: wy_ref[c, b, p, pl.ds(j0, step), :],
            )
            for d in range(2):
                w_re = [sources[d](0, b).astype(jnp.float32) for b in range(3)]
                w_im = [sources[d](1, b).astype(jnp.float32) for b in range(3)]
                for a in range(3):
                    re = None
                    im = None
                    for b in range(3):
                        k = d * 18 + a * 3 + b
                        gr = g_ref[p, k : k + 1, :]
                        gi = g_ref[p, k + 9 : k + 10, :]
                        t_re = gr * w_re[b] - gi * w_im[b]
                        t_im = gr * w_im[b] + gi * w_re[b]
                        re = t_re if re is None else re + t_re
                        im = t_im if im is None else im + t_im
                    r_ref[pl.ds(2 * d * vecs + j0, step), lanes(p, a)] = re.astype(jnp.bfloat16)
                    r_ref[pl.ds((2 * d + 1) * vecs + j0, step), lanes(p, a)] = im.astype(jnp.bfloat16)
            return inner_carry

        lax.fori_loop(0, vecs // step, rows_block, 0)
        return carry

    lax.fori_loop(0, planes, plane, 0)
    used = planes * span
    stacked = vt_ref[:, :, 0:used].reshape(2 * vecs, used)
    both = lax.dot_general(r_ref[...], stacked, nt, preferred_element_type=jnp.float32)
    for d in range(2):
        o = 2 * d * vecs
        real = both[o : o + vecs, 0:vecs] + both[o + vecs : o + 2 * vecs, vecs : 2 * vecs]
        imag = both[o + vecs : o + 2 * vecs, 0:vecs] - both[o : o + vecs, vecs : 2 * vecs]
        o_ref[d, 0] = real.T * scaling
        o_ref[d, 1] = imag.T * scaling


def site_rows(gauge_x, gauge_y):
    nx, ny, nz = gauge_x.shape[3:]
    both = jnp.concatenate([gauge_x.reshape(18, nx, ny * nz), gauge_y.reshape(18, nx, ny * nz)], 0)
    return jnp.transpose(both, (1, 0, 2))


def partials(vectors, from_next_x, from_next_y, gauge_x, gauge_y, scaling):
    nx, ny, nz, nv = vectors.shape[2:]
    sites = ny * nz
    vmem = pltpu.MemorySpace.VMEM
    inner = pl.pallas_call(
        lambda *refs: elementals_kernel(scaling, *refs),
        out_shape=jax.ShapeDtypeStruct((2, 2, nv, nv), jnp.float32),
        in_specs=[pl.BlockSpec(memory_space=vmem)] * 2,
        out_specs=pl.BlockSpec(memory_space=vmem),
        scratch_shapes=[
            pltpu.VMEM((2, nv, (nx + 1) * 3 * sites), jnp.bfloat16),
            pltpu.VMEM((2, 3, nx, nv, sites), jnp.bfloat16),
            pltpu.VMEM((4 * nv, nx * 3 * sites), jnp.bfloat16),
        ],
    )(vectors, site_rows(gauge_x, gauge_y))
    inner, from_next_x, from_next_y = lax.optimization_barrier((inner, from_next_x, from_next_y))
    edges = jnp.stack(
        [
            last_term(vectors[:, :, nx - 1 :], from_next_x, gauge_x[:, :, :, nx - 1 :], scaling),
            last_term(vectors[:, :, :, ny - 1 :], from_next_y, gauge_y[:, :, :, :, ny - 1 :], scaling),
        ]
    )
    return inner + edges


def colour_apply(gauge, source_vectors):
    real_parts = []
    imag_parts = []
    for colour in range(3):
        real_running = jnp.zeros(source_vectors.shape[2:], jnp.float32)
        imaginary_running = jnp.zeros(source_vectors.shape[2:], jnp.float32)
        for inner_product in range(3):
            left_real = gauge[0, colour, inner_product][..., None]
            left_imaginary = gauge[1, colour, inner_product][..., None]
            right_real = source_vectors[0, inner_product].astype(jnp.float32)
            right_imaginary = source_vectors[1, inner_product].astype(jnp.float32)
            real_running = real_running + left_real * right_real - left_imaginary * right_imaginary
            imaginary_running = (
                imaginary_running + left_real * right_imaginary + left_imaginary * right_real
            )
        real_parts.append(real_running)
        imag_parts.append(imaginary_running)
    return jnp.stack([jnp.stack(real_parts), jnp.stack(imag_parts)]).astype(jnp.bfloat16)


def last_term(left_vectors, source, gauge, scaling):
    nv = left_vectors.shape[-1]
    image = colour_apply(gauge, source)
    left = left_vectors.reshape(-1, nv)
    right_re = image[0].reshape(-1, nv)
    right_im = image[1].reshape(-1, nv)
    right = jnp.concatenate(
        [jnp.concatenate([right_re, right_im], 1), jnp.concatenate([right_im, -right_re], 1)], 0
    )
    dims = (((0,), (0,)), ((), ()))
    both = lax.dot_general(left, right, dims, preferred_element_type=jnp.float32)
    return both.reshape(nv, 2, nv).transpose(1, 0, 2) * scaling


def reduce_partials(x):
    shape = x.shape
    n = lax.axis_size("gx") * lax.axis_size("yz")
    chunks = x.reshape(n, -1, shape[-1])
    got = lax.all_to_all(chunks, ("gx", "yz"), 0, 0, tiled=True)
    total = jnp.sum(got, 0, keepdims=True)
    every = jnp.broadcast_to(total, chunks.shape)
    return lax.all_to_all(every, ("gx", "yz"), 0, 0, tiled=True).reshape(shape)


def local(vectors, gauge_x, gauge_y):
    from_next_x = shifted(vectors[:, :, :1], "gx", -1)
    from_next_y = shifted(vectors[:, :, :, :1], "yz", -1)
    sites_total = (
        vectors.shape[2]
        * lax.axis_size("gx")
        * vectors.shape[3]
        * lax.axis_size("yz")
        * vectors.shape[4]
    )
    scaling = 1.0 / math.sqrt(3.0 * sites_total)
    return reduce_partials(partials(vectors, from_next_x, from_next_y, gauge_x, gauge_y, scaling))


def solution(mesh):
    placed = (
        P(None, None, "gx", "yz", "ta", None),
        P(None, None, None, "gx", "yz", "ta"),
        P(None, None, None, "gx", "yz", "ta"),
    )
    return jax.shard_map(
        local, mesh=mesh, in_specs=placed, out_specs=P("ta", None, None, None), check_vma=False
    )
```

```python
import math

import jax
import jax.numpy as jnp
from jax import lax
from jax.experimental import pallas as pl
from jax.experimental.pallas import tpu as pltpu
from jax.sharding import PartitionSpec as P


def shifted(value, axis, steps):
    count = lax.axis_size(axis)
    pairs = [(source, (source + steps) % count) for source in range(count)]
    return lax.ppermute(value, axis, pairs)


def elementals_kernel(scaling, v_ref, g_ref, o_ref, vt_ref, wy_ref, r_ref):
    planes, lines, row, vecs = v_ref.shape[2:]
    sites = lines * row
    span = 3 * sites
    step = 16
    nt = (((1,), (1,)), ((), ()))

    def lanes(p, a):
        return pl.ds(pl.multiple_of(p * span + a * sites, sites), sites)

    def transpose_plane(p, carry):
        for c in range(2):
            for a in range(3):
                vt_ref[c, :, lanes(p, a)] = v_ref[c, a, p].reshape(sites, vecs).T
                inner = v_ref[c, a, p, 1:].reshape(sites - row, vecs)
                edge = jnp.zeros((row, vecs), inner.dtype)
                wy_ref[c, a, p] = jnp.concatenate([inner, edge], 0).T
        return carry

    lax.fori_loop(0, planes, transpose_plane, 0, unroll=2)
    for c in range(2):
        for a in range(3):
            vt_ref[c, :, lanes(planes, a)] = jnp.zeros((vecs, sites), vt_ref.dtype)

    def plane(p, carry):
        def rows_block(jc, inner_carry):
            j0 = pl.multiple_of(jc * step, step)
            sources = (
                lambda c, b: vt_ref[c, pl.ds(j0, step), lanes(p + 1, b)],
                lambda c, b: wy_ref[c, b, p, pl.ds(j0, step), :],
            )
            for d in range(2):
                w_re = [sources[d](0, b).astype(jnp.float32) for b in range(3)]
                w_im = [sources[d](1, b).astype(jnp.float32) for b in range(3)]
                for a in range(3):
                    re = None
                    im = None
                    for b in range(3):
                        k = d * 18 + a * 3 + b
                        gr = g_ref[p, k : k + 1, :]
                        gi = g_ref[p, k + 9 : k + 10, :]
                        t_re = gr * w_re[b] - gi * w_im[b]
                        t_im = gr * w_im[b] + gi * w_re[b]
                        re = t_re if re is None else re + t_re
                        im = t_im if im is None else im + t_im
                    r_ref[pl.ds(2 * d * vecs + j0, step), lanes(p, a)] = re.astype(jnp.bfloat16)
                    r_ref[pl.ds((2 * d + 1) * vecs + j0, step), lanes(p, a)] = im.astype(jnp.bfloat16)
            return inner_carry

        lax.fori_loop(0, vecs // step, rows_block, 0, unroll=2)
        return carry

    lax.fori_loop(0, planes, plane, 0)
    used = planes * span
    stacked = vt_ref[:, :, 0:used].reshape(2 * vecs, used)
    both = lax.dot_general(r_ref[...], stacked, nt, preferred_element_type=jnp.float32)
    for d in range(2):
        o = 2 * d * vecs
        real = both[o : o + vecs, 0:vecs] + both[o + vecs : o + 2 * vecs, vecs : 2 * vecs]
        imag = both[o + vecs : o + 2 * vecs, 0:vecs] - both[o : o + vecs, vecs : 2 * vecs]
        o_ref[d, 0] = real.T * scaling
        o_ref[d, 1] = imag.T * scaling


def site_rows(gauge_x, gauge_y):
    nx, ny, nz = gauge_x.shape[3:]
    both = jnp.concatenate([gauge_x.reshape(18, nx, ny * nz), gauge_y.reshape(18, nx, ny * nz)], 0)
    return jnp.transpose(both, (1, 0, 2))


def partials(vectors, from_next_x, from_next_y, gauge_x, gauge_y, scaling):
    nx, ny, nz, nv = vectors.shape[2:]
    sites = ny * nz
    vmem = pltpu.MemorySpace.VMEM
    inner = pl.pallas_call(
        lambda *refs: elementals_kernel(scaling, *refs),
        out_shape=jax.ShapeDtypeStruct((2, 2, nv, nv), jnp.float32),
        in_specs=[pl.BlockSpec(memory_space=vmem)] * 2,
        out_specs=pl.BlockSpec(memory_space=vmem),
        scratch_shapes=[
            pltpu.VMEM((2, nv, (nx + 1) * 3 * sites), jnp.bfloat16),
            pltpu.VMEM((2, 3, nx, nv, sites), jnp.bfloat16),
            pltpu.VMEM((4 * nv, nx * 3 * sites), jnp.bfloat16),
        ],
    )(vectors, site_rows(gauge_x, gauge_y))
    inner, from_next_x, from_next_y = lax.optimization_barrier((inner, from_next_x, from_next_y))
    edges = jnp.stack(
        [
            last_term(vectors[:, :, nx - 1 :], from_next_x, gauge_x[:, :, :, nx - 1 :], scaling),
            last_term(vectors[:, :, :, ny - 1 :], from_next_y, gauge_y[:, :, :, :, ny - 1 :], scaling),
        ]
    )
    return inner + edges


def colour_apply(gauge, source_vectors):
    real_parts = []
    imag_parts = []
    for colour in range(3):
        real_running = jnp.zeros(source_vectors.shape[2:], jnp.float32)
        imaginary_running = jnp.zeros(source_vectors.shape[2:], jnp.float32)
        for inner_product in range(3):
            left_real = gauge[0, colour, inner_product][..., None]
            left_imaginary = gauge[1, colour, inner_product][..., None]
            right_real = source_vectors[0, inner_product].astype(jnp.float32)
            right_imaginary = source_vectors[1, inner_product].astype(jnp.float32)
            real_running = real_running + left_real * right_real - left_imaginary * right_imaginary
            imaginary_running = (
                imaginary_running + left_real * right_imaginary + left_imaginary * right_real
            )
        real_parts.append(real_running)
        imag_parts.append(imaginary_running)
    return jnp.stack([jnp.stack(real_parts), jnp.stack(imag_parts)]).astype(jnp.bfloat16)


def last_term(left_vectors, source, gauge, scaling):
    nv = left_vectors.shape[-1]
    image = colour_apply(gauge, source)
    left = left_vectors.reshape(-1, nv)
    right_re = image[0].reshape(-1, nv)
    right_im = image[1].reshape(-1, nv)
    right = jnp.concatenate(
        [jnp.concatenate([right_re, right_im], 1), jnp.concatenate([right_im, -right_re], 1)], 0
    )
    dims = (((0,), (0,)), ((), ()))
    both = lax.dot_general(left, right, dims, preferred_element_type=jnp.float32)
    return both.reshape(nv, 2, nv).transpose(1, 0, 2) * scaling


def reduce_partials(x):
    shape = x.shape
    n = lax.axis_size("gx") * lax.axis_size("yz")
    chunks = x.reshape(n, -1, shape[-1])
    got = lax.all_to_all(chunks, ("gx", "yz"), 0, 0, tiled=True)
    total = jnp.sum(got, 0, keepdims=True)
    every = jnp.broadcast_to(total, chunks.shape)
    return lax.all_to_all(every, ("gx", "yz"), 0, 0, tiled=True).reshape(shape)


def local(vectors, gauge_x, gauge_y):
    from_next_x = shifted(vectors[:, :, :1], "gx", -1)
    from_next_y = shifted(vectors[:, :, :, :1], "yz", -1)
    sites_total = (
        vectors.shape[2]
        * lax.axis_size("gx")
        * vectors.shape[3]
        * lax.axis_size("yz")
        * vectors.shape[4]
    )
    scaling = 1.0 / math.sqrt(3.0 * sites_total)
    return reduce_partials(partials(vectors, from_next_x, from_next_y, gauge_x, gauge_y, scaling))


def solution(mesh):
    placed = (
        P(None, None, "gx", "yz", "ta", None),
        P(None, None, None, "gx", "yz", "ta"),
        P(None, None, None, "gx", "yz", "ta"),
    )
    return jax.shard_map(
        local, mesh=mesh, in_specs=placed, out_specs=P("ta", None, None, None), check_vma=False
    )
```
